32 devices in a mesh: clu: 8 (over z, y), rhs: 4 (over x, core).
Axes of the slice: x: 2, y: 2, z: 4, core: 2. Of those that a mesh axis runs over, the one named last changes fastest.
Arguments:
- rhs: float32 [8, 8, 16, 128], P(None, 'clu', 'rhs'), parts along dimension 2, may hold values from -6 to 6
- inverse: float32 [8, 8, 128, 128], P(None, 'clu'), as said below
- lower_blocks: float32 [8, 8, 4, 128, 128], P(None, 'clu'), may hold values from -0.125 to 0.125
- upper_blocks: float32 [8, 8, 4, 128, 128], P(None, 'clu'), may hold values from -0.125 to 0.125
- lower_cols: int32 [8, 8, 4], P(None, 'clu'), may hold values from -1 to 63, as said below
- upper_cols: int32 [8, 8, 4], P(None, 'clu'), may hold values from -1 to 63, as said below
- levels: int32 [8, 8], P(None, 'clu'), may hold values from 0 to 3, as said below
Outputs:
- solution: float32 [8, 8, 16, 128], P(None, 'clu', 'rhs'), parts along dimension 2
The draws below stay inside these ranges and needn't reach their ends.
There are 4 independent parts, one for each index of `rhs`. The reference program is written for one: setup_inputs(seed, part) draws one part's arguments, and reference() takes and returns one part's arrays. A program takes and returns all parts, laid end to end along the dimension named above; an argument that names none is the same for every part. Nothing has to cross between parts.
Inputs may be any that keep to these rules, and one draw needn't show every extreme that they name: `levels`: every device holds exactly 3 clusters of one level and at least one cluster of every level; which level is the full one differs from device to device. `lower_cols`: every block of a cluster of level 0 is -1; every block of any other cluster names a cluster of a lower level. `upper_cols`: every block of a cluster of level 3 is -1; every block of any other cluster names a cluster of a higher level. `inverse`: each block has full rank.
All inputs are finite; a program needn't handle non-finite values.
Results may differ from the reference program's by a relative error of at most 0.0001.
Values sent between devices are 32-bit elements; how exact they have to be, the bound alone decides.
No kernel may reach another device: no remote copies, remote signals or barrier semaphores. Data moves between devices by JAX's collectives and lax.ppermute only.
A program may use at most 64 MiB of HBM per device.

```python
import math
import jax
import jax.numpy as jnp
import numpy as np
from jax import lax

P_SIZE = 128
R = 4
CL_DEV = 8
LEVELS = 4
KL = 4
KU = 4
NC = 64
N_CLU = 8


def pick_columns(section_map, key, count, downward):
    dev_count = section_map.shape[1]
    key_target, key_peer, key_score = jax.random.split(key, 3)
    dims_all = (CL_DEV, dev_count, count)
    own_level = section_map[:, :, None]
    if downward:
        reach = jnp.maximum(own_level, 1)
        target = jax.random.randint(key_target, dims_all, 0, reach)
        present = own_level > 0
    else:
        reach = jnp.maximum(LEVELS - 1 - own_level, 1)
        target = own_level + 1 + jax.random.randint(key_target, dims_all, 0, reach)
        present = own_level < LEVELS - 1
    peer_dev = jax.random.randint(key_peer, dims_all, 0, dev_count)
    candidate = section_map.T[peer_dev]
    scores = jax.random.randint(key_score, dims_all + (CL_DEV,), 0, 65536) * CL_DEV + jnp.arange(CL_DEV)[None, None, None, :] + 1
    scores = jnp.where(candidate == target[..., None], scores, 0)
    local_idx = jnp.argmax(scores, axis=-1).astype(jnp.int32)
    column = local_idx * dev_count + peer_dev
    return jnp.where(present, column, -1).astype(jnp.int32)


def structure(key):
    dev_count = NC // CL_DEV
    base_count = CL_DEV // LEVELS
    counts_list = [base_count + 1] + [base_count] * (LEVELS - 2) + [base_count - 1]
    order_table = np.repeat(np.arange(LEVELS), counts_list)
    key_level = jax.random.fold_in(key, 101)
    key_slot = jax.random.fold_in(key, 202)
    key_lower = jax.random.fold_in(key, 303)
    key_upper = jax.random.fold_in(key, 404)
    perm_level = jax.vmap(lambda item: jax.random.permutation(item, LEVELS))(jax.random.split(key_level, dev_count))
    perm_slot = jax.vmap(lambda item: jax.random.permutation(item, CL_DEV))(jax.random.split(key_slot, dev_count))
    sorted_level = perm_level[:, order_table].astype(jnp.int32)
    dev_rows = jnp.arange(dev_count)[:, None]
    level_dev = jnp.zeros((dev_count, CL_DEV), jnp.int32).at[dev_rows, perm_slot].set(sorted_level)
    section_map = level_dev.T
    lower = pick_columns(section_map, key_lower, KL, True)
    upper = pick_columns(section_map, key_upper, KU, False)
    return (section_map, lower, upper)


def draw_levels(key, part):
    return structure(key)[0]


def draw_lower_cols(key, part):
    return structure(key)[1]


def draw_upper_cols(key, part):
    return structure(key)[2]


def draw_inverse(key, part):
    key_diag, key_off = jax.random.split(key, 2)
    dims_all = (CL_DEV, NC // CL_DEV, P_SIZE)
    diagonal = jnp.exp(jax.random.uniform(key_diag, dims_all, jnp.float32, math.log(0.5), math.log(2.0)))
    spread = jax.random.normal(key_off, dims_all + (P_SIZE,), jnp.float32) * (0.35 / math.sqrt(P_SIZE))
    matrix = spread + jnp.eye(P_SIZE, dtype=jnp.float32) * diagonal[..., :, None]
    return matrix.astype(jnp.float32)


def level_of(key, shape, cuts, low, top_value):
    loudness = 1.0
    for position, parts in cuts:
        heights = jax.random.uniform(jax.random.fold_in(jax.random.fold_in(key, 6), position), (parts,), jnp.float32, low / len(cuts), top_value / len(cuts))
        loudness = loudness * jnp.repeat(jnp.exp(heights), shape[position] // parts).reshape((-1,) + (1,) * (len(shape) - 1 - position))
    return loudness


def bell_draw(stream_key, extent, scale, limit, cuts=(), kind=jnp.bfloat16):
    values = scale * jax.random.normal(stream_key, extent, jnp.float32)
    if cuts:
        values = values * level_of(stream_key, extent, cuts, -0.22, 0.18)
    return jnp.clip(values, -limit, limit).astype(kind)


def setup_inputs(seed: int = 0, part: int = 0) -> dict:
    keys = jax.random.split(jax.random.key(seed), 8)
    own_keys = jax.random.split(jax.random.fold_in(keys[7], part), 8)
    rhs = bell_draw(own_keys[0], (CL_DEV, N_CLU, R, P_SIZE), 1.0, 6.0, ((1, 8),), jnp.float32)
    inverse = draw_inverse(jax.random.fold_in(keys[7], 71), part)
    lower_blocks = bell_draw(keys[2], (CL_DEV, N_CLU, KL, P_SIZE, P_SIZE), (16 * P_SIZE) ** -0.5, 0.125, ((1, 8),), jnp.float32)
    upper_blocks = bell_draw(keys[3], (CL_DEV, N_CLU, KU, P_SIZE, P_SIZE), (16 * P_SIZE) ** -0.5, 0.125, ((1, 8),), jnp.float32)
    lower_cols = draw_lower_cols(jax.random.fold_in(keys[7], 71), part)
    upper_cols = draw_upper_cols(jax.random.fold_in(keys[7], 71), part)
    levels = draw_levels(jax.random.fold_in(keys[7], 71), part)
    return dict(rhs=rhs, inverse=inverse, lower_blocks=lower_blocks, upper_blocks=upper_blocks, lower_cols=lower_cols, upper_cols=upper_cols, levels=levels)


def gather_blocks(blocks, columns, values):
    present = columns >= 0
    picked = values[jnp.where(present, columns, 0)]
    picked = jnp.where(present[..., None, None], picked, jnp.zeros_like(picked))
    return jnp.einsum("ckpq,ckrq->crp", blocks, picked, precision=lax.Precision.HIGHEST)


def reference(rhs, inverse, lower_blocks, upper_blocks, lower_cols, upper_cols, levels):
    clusters = CL_DEV * N_CLU
    source = rhs.reshape(clusters, R, P_SIZE)
    inv_flat = inverse.reshape(clusters, P_SIZE, P_SIZE)
    low_flat = lower_blocks.reshape(clusters, KL, P_SIZE, P_SIZE)
    up_flat = upper_blocks.reshape(clusters, KU, P_SIZE, P_SIZE)
    low_cols = lower_cols.reshape(clusters, KL)
    up_cols = upper_cols.reshape(clusters, KU)
    sections = levels.reshape(clusters)

    def solve_diag(values):
        return jnp.einsum("cpq,crq->crp", inv_flat, values, precision=lax.Precision.HIGHEST)

    forward = source
    for level_no in range(1, LEVELS):
        update = source - gather_blocks(low_flat, low_cols, forward)
        forward = jnp.where((sections == level_no)[:, None, None], update, forward)
    backward = solve_diag(forward)
    backward = jnp.where((sections == LEVELS - 1)[:, None, None], backward, jnp.zeros_like(backward))
    for level_no in range(LEVELS - 2, -1, -1):
        update = solve_diag(forward - gather_blocks(up_flat, up_cols, backward))
        backward = jnp.where((sections == level_no)[:, None, None], update, backward)
    return backward.reshape(CL_DEV, N_CLU, R, P_SIZE)
```

```python
import jax
import jax.numpy as jnp
from jax import lax
from jax.sharding import PartitionSpec as P

LEVELS = 4


def gather_blocks(blocks, columns, table):
    dev_count = table.shape[0]
    present = columns >= 0
    safe = jnp.where(present, columns, 0)
    picked = table[safe % dev_count, safe // dev_count]
    picked = jnp.where(present[..., None, None], picked, jnp.zeros_like(picked))
    return jnp.einsum("ckpq,ckrq->crp", blocks, picked, precision=lax.Precision.HIGHEST)


def solve_diag(inv_local, values):
    return jnp.einsum("cpq,crq->crp", inv_local, values, precision=lax.Precision.HIGHEST)


def per_device(rhs, inverse, lower_blocks, upper_blocks, lower_cols, upper_cols, levels):
    dev_count = lax.axis_size("clu")
    source = rhs[:, 0]
    inv_local = inverse[:, 0]
    low_local = lower_blocks[:, 0]
    up_local = upper_blocks[:, 0]
    low_cols = lower_cols[:, 0]
    up_cols = upper_cols[:, 0]
    sections = levels[:, 0]

    def share(values):
        spread = jnp.broadcast_to(values[None], (dev_count,) + values.shape)
        return lax.all_to_all(spread, "clu", 0, 0, tiled=False)

    forward = source
    for level_no in range(1, LEVELS):
        table = share(forward)
        update = source - gather_blocks(low_local, low_cols, table)
        forward = jnp.where((sections == level_no)[:, None, None], update, forward)
    backward = solve_diag(inv_local, forward)
    backward = jnp.where(
        (sections == LEVELS - 1)[:, None, None], backward, jnp.zeros_like(backward)
    )
    for level_no in range(LEVELS - 2, -1, -1):
        table = share(backward)
        update = solve_diag(inv_local, forward - gather_blocks(up_local, up_cols, table))
        backward = jnp.where((sections == level_no)[:, None, None], update, backward)
    return backward[:, None]


def solution(mesh):
    return jax.shard_map(
        per_device,
        mesh=mesh,
        in_specs=(
            P(None, "clu", "rhs", None),
            P(None, "clu", None, None),
            P(None, "clu", None, None, None),
            P(None, "clu", None, None, None),
            P(None, "clu", None),
            P(None, "clu", None),
            P(None, "clu"),
        ),
        out_specs=P(None, "clu", "rhs", None),
        check_vma=False,
    )
```

```python
import functools

import jax
import jax.numpy as jnp
from jax import lax
from jax.experimental import pallas as pl
from jax.experimental.pallas import tpu as pltpu
from jax.sharding import PartitionSpec as P

LEVELS = 4
HIGHEST = lax.Precision.HIGHEST


def _nt(a, b):
    return lax.dot_general(a, b, (((1,), (1,)), ((), ())), precision=HIGHEST,
                           preferred_element_type=jnp.float32)


def _level_kernel(level, n_dev, mode, cols_ref, lev_ref, table_ref, base_ref, prev_ref,
                  blk_hbm, inv_hbm, *rest):
    if mode == "last":
        out_ref, sol_ref, buf, ibuf, sem, isem, acc_ref = rest
    else:
        out_ref, buf, ibuf, sem, isem, acc_ref = rest
    n_cl, n_k = buf.shape[0], buf.shape[1]
    solve = mode != "fwd"

    def blk_copy(c, k):
        return pltpu.make_async_copy(blk_hbm.at[c, k], buf.at[c, k], sem.at[c, k])

    def inv_copy(c):
        return pltpu.make_async_copy(inv_hbm.at[c], ibuf.at[c], isem.at[c])

    for c in range(n_cl):
        @pl.when(lev_ref[c] == level)
        def _():
            for k in range(n_k):
                @pl.when(cols_ref[c * n_k + k] >= 0)
                def _():
                    blk_copy(c, k).start()
            if solve:
                inv_copy(c).start()

    out_ref[...] = prev_ref[...]
    if mode == "last":
        sol_ref[...] = jnp.zeros(sol_ref.shape, sol_ref.dtype)

    for c in range(n_cl):
        @pl.when(lev_ref[c] == level)
        def _():
            acc_ref[...] = base_ref[c]
            for k in range(n_k):
                j = cols_ref[c * n_k + k]

                @pl.when(j >= 0)
                def _():
                    blk_copy(c, k).wait()
                    picked = table_ref[j % n_dev, j // n_dev]
                    acc_ref[...] = acc_ref[...] - _nt(picked, buf[c, k])
            if mode == "fwd":
                out_ref[c] = acc_ref[...]
            else:
                inv_copy(c).wait()
                solved = _nt(acc_ref[...], ibuf[c])
                if mode == "last":
                    out_ref[c] = acc_ref[...]
                    sol_ref[c] = solved
                else:
                    out_ref[c] = solved


def level_step(level, mode, cols, lev, table, base, prev, blocks, inverse):
    n_dev = table.shape[0]
    n_cl, n_k, p_size = blocks.shape[0], blocks.shape[1], blocks.shape[2]
    vec = jax.ShapeDtypeStruct(base.shape, jnp.float32)
    out_shape = (vec, vec) if mode == "last" else vec
    smem = pl.BlockSpec(memory_space=pltpu.SMEM)
    vmem = pl.BlockSpec(memory_space=pltpu.VMEM)
    hbm = pl.BlockSpec(memory_space=pl.ANY)
    kernel = functools.partial(_level_kernel, level, n_dev, mode)
    return pl.pallas_call(
        kernel,
        out_shape=out_shape,
        in_specs=[smem, smem, vmem, vmem, vmem, hbm, hbm],
        out_specs=(vmem, vmem) if mode == "last" else vmem,
        scratch_shapes=[
            pltpu.VMEM(blocks.shape, jnp.float32),
            pltpu.VMEM(inverse.shape, jnp.float32),
            pltpu.SemaphoreType.DMA((n_cl, n_k)),
            pltpu.SemaphoreType.DMA((n_cl,)),
            pltpu.VMEM(base.shape[1:], jnp.float32),
        ],
    )(cols, lev, table, base, prev, blocks, inverse)


def per_device(rhs, inverse, lower_blocks, upper_blocks, lower_cols, upper_cols, levels):
    dev_count = lax.axis_size("clu")
    source = rhs[:, 0]
    inv_local = inverse[:, 0]
    low_local = lower_blocks[:, 0]
    up_local = upper_blocks[:, 0]
    low_cols = lower_cols[:, 0].reshape(-1)
    up_cols = upper_cols[:, 0].reshape(-1)
    sections = levels[:, 0]

    def share(values):
        spread = jnp.broadcast_to(values[None], (dev_count,) + values.shape)
        return lax.all_to_all(spread, "clu", 0, 0, tiled=False)

    forward = source
    for level_no in range(1, LEVELS - 1):
        forward = level_step(level_no, "fwd", low_cols, sections, share(forward), source,
                             forward, low_local, inv_local)
    forward, backward = level_step(LEVELS - 1, "last", low_cols, sections, share(forward),
                                   source, forward, low_local, inv_local)
    for level_no in range(LEVELS - 2, -1, -1):
        backward = level_step(level_no, "bwd", up_cols, sections, share(backward), forward,
                              backward, up_local, inv_local)
    return backward[:, None]


def solution(mesh):
    return jax.shard_map(
        per_device,
        mesh=mesh,
        in_specs=(
            P(None, "clu", "rhs", None),
            P(None, "clu", None, None),
            P(None, "clu", None, None, None),
            P(None, "clu", None, None, None),
            P(None, "clu", None),
            P(None, "clu", None),
            P(None, "clu"),
        ),
        out_specs=P(None, "clu", "rhs", None),
        check_vma=False,
    )
```

```python
import functools

import jax
import jax.numpy as jnp
from jax import lax
from jax.experimental import pallas as pl
from jax.experimental.pallas import tpu as pltpu
from jax.sharding import PartitionSpec as P

LEVELS = 4
SLOTS = 3
HIGHEST = lax.Precision.HIGHEST


def _nt(a, b):
    return lax.dot_general(a, b, (((1,), (1,)), ((), ())), precision=HIGHEST,
                           preferred_element_type=jnp.float32)


def _level_kernel(level, n_dev, mode, spread, cols_ref, lev_ref, table_ref, base_ref,
                  prev_ref, blk_hbm, inv_hbm, *rest):
    rest = list(rest)
    out_ref = rest.pop(0)
    sol_ref = rest.pop(0) if mode == "last" else None
    spread_ref = rest.pop(0) if spread else None
    buf, ibuf, sem, isem, sel_ref = rest
    n_cl = prev_ref.shape[0]
    n_k = buf.shape[1]
    solve = mode != "fwd"

    for s in range(SLOTS):
        sel_ref[s] = 0
    count = jnp.int32(0)
    for c in range(n_cl):
        hit = lev_ref[c] == level

        @pl.when(hit)
        def _():
            sel_ref[jnp.minimum(count, SLOTS - 1)] = c

        count = count + hit.astype(jnp.int32)

    copies = []
    inv_copies = []
    for s in range(SLOTS):
        c = sel_ref[s]
        row = []
        for k in range(n_k):
            cp = pltpu.make_async_copy(blk_hbm.at[c, k], buf.at[s, k], sem.at[s, k])
            cp.start()
            row.append(cp)
        copies.append(row)
        if solve:
            cp = pltpu.make_async_copy(inv_hbm.at[c], ibuf.at[s], isem.at[s])
            cp.start()
            inv_copies.append(cp)

    out_ref[...] = prev_ref[...]
    if mode == "last":
        sol_ref[...] = jnp.zeros(sol_ref.shape, sol_ref.dtype)

    results = []
    for s in range(SLOTS):
        c = sel_ref[s]
        acc = base_ref[c]
        for k in range(n_k):
            j = cols_ref[c * n_k + k]
            jj = jnp.maximum(j, 0)
            picked = table_ref[jj % n_dev, jj // n_dev]
            picked = jnp.where(j >= 0, picked, jnp.zeros_like(picked))
            copies[s][k].wait()
            acc = acc - _nt(picked, buf[s, k])
        solved = None
        if solve:
            inv_copies[s].wait()
            solved = _nt(acc, ibuf[s])
        results.append((c, acc, solved))

    for s, (c, acc, solved) in enumerate(results):
        @pl.when(s < count)
        def _():
            if mode == "fwd":
                out_ref[c] = acc
            elif mode == "last":
                out_ref[c] = acc
                sol_ref[c] = solved
            else:
                out_ref[c] = solved

    if spread:
        shared = sol_ref if mode == "last" else out_ref

        def body(d, carry):
            spread_ref[d] = shared[...]
            return carry

        lax.fori_loop(0, n_dev, body, 0)


def level_step(level, mode, spread, n_dev, cols, lev, table, base, prev, blocks, inverse):
    n_k, p_size = blocks.shape[1], blocks.shape[2]
    vec = jax.ShapeDtypeStruct(base.shape, jnp.float32)
    outs = [vec]
    if mode == "last":
        outs.append(vec)
    if spread:
        outs.append(jax.ShapeDtypeStruct((n_dev,) + base.shape, jnp.float32))
    smem = pl.BlockSpec(memory_space=pltpu.SMEM)
    vmem = pl.BlockSpec(memory_space=pltpu.VMEM)
    hbm = pl.BlockSpec(memory_space=pl.ANY)
    kernel = functools.partial(_level_kernel, level, n_dev, mode, spread)
    return pl.pallas_call(
        kernel,
        out_shape=tuple(outs),
        in_specs=[smem, smem, vmem, vmem, vmem, hbm, hbm],
        out_specs=tuple(vmem for _ in outs),
        scratch_shapes=[
            pltpu.VMEM((SLOTS, n_k, p_size, p_size), jnp.float32),
            pltpu.VMEM((SLOTS, p_size, p_size), jnp.float32),
            pltpu.SemaphoreType.DMA((SLOTS, n_k)),
            pltpu.SemaphoreType.DMA((SLOTS,)),
            pltpu.SMEM((SLOTS,), jnp.int32),
        ],
    )(cols, lev, table, base, prev, blocks, inverse)


def per_device(rhs, inverse, lower_blocks, upper_blocks, lower_cols, upper_cols, levels):
    n_dev = lax.axis_size("clu")
    source = rhs[:, 0]
    inv_local = inverse[:, 0]
    low_local = lower_blocks[:, 0]
    up_local = upper_blocks[:, 0]
    low_cols = lower_cols[:, 0].reshape(-1)
    up_cols = upper_cols[:, 0].reshape(-1)
    sections = levels[:, 0]

    def share(spread):
        return lax.all_to_all(spread, "clu", 0, 0, tiled=False)

    spread = jnp.broadcast_to(source[None], (n_dev,) + source.shape)
    forward = source
    for level_no in range(1, LEVELS - 1):
        forward, spread = level_step(level_no, "fwd", True, n_dev, low_cols, sections,
                                     share(spread), source, forward, low_local, inv_local)
    forward, backward, spread = level_step(LEVELS - 1, "last", True, n_dev, low_cols,
                                           sections, share(spread), source, forward,
                                           low_local, inv_local)
    for level_no in range(LEVELS - 2, -1, -1):
        last = level_no == 0
        res = level_step(level_no, "bwd", not last, n_dev, up_cols, sections, share(spread),
                         forward, backward, up_local, inv_local)
        if last:
            (backward,) = res
        else:
            backward, spread = res
    return backward[:, None]


def solution(mesh):
    return jax.shard_map(
        per_device,
        mesh=mesh,
        in_specs=(
            P(None, "clu", "rhs", None),
            P(None, "clu", None, None),
            P(None, "clu", None, None, None),
            P(None, "clu", None, None, None),
            P(None, "clu", None),
            P(None, "clu", None),
            P(None, "clu"),
        ),
        out_specs=P(None, "clu", "rhs", None),
        check_vma=False,
    )
```

```python
import jax
import jax.numpy as jnp
from jax import lax
from jax.sharding import PartitionSpec as P

LEVELS = 4


def gather_blocks(blocks, columns, table):
    dev_count = table.shape[0]
    present = columns >= 0
    safe = jnp.where(present, columns, 0)
    picked = table[safe % dev_count, safe // dev_count]
    picked = jnp.where(present[..., None, None], picked, jnp.zeros_like(picked))
    return jnp.einsum("ckpq,ckrq->crp", blocks, picked, precision=lax.Precision.HIGH)


def solve_diag(inv_local, values):
    return jnp.einsum("cpq,crq->crp", inv_local, values, precision=lax.Precision.HIGH)


def per_device(rhs, inverse, lower_blocks, upper_blocks, lower_cols, upper_cols, levels):
    dev_count = lax.axis_size("clu")
    source = rhs[:, 0]
    inv_local = inverse[:, 0]
    low_local = lower_blocks[:, 0]
    up_local = upper_blocks[:, 0]
    low_cols = lower_cols[:, 0]
    up_cols = upper_cols[:, 0]
    sections = levels[:, 0]

    def share(values):
        spread = jnp.broadcast_to(values[None], (dev_count,) + values.shape)
        return lax.all_to_all(spread, "clu", 0, 0, tiled=False)

    forward = source
    for level_no in range(1, LEVELS):
        table = share(forward)
        update = source - gather_blocks(low_local, low_cols, table)
        forward = jnp.where((sections == level_no)[:, None, None], update, forward)
    backward = solve_diag(inv_local, forward)
    backward = jnp.where(
        (sections == LEVELS - 1)[:, None, None], backward, jnp.zeros_like(backward)
    )
    for level_no in range(LEVELS - 2, -1, -1):
        table = share(backward)
        update = solve_diag(inv_local, forward - gather_blocks(up_local, up_cols, table))
        backward = jnp.where((sections == level_no)[:, None, None], update, backward)
    return backward[:, None]


def solution(mesh):
    return jax.shard_map(
        per_device,
        mesh=mesh,
        in_specs=(
            P(None, "clu", "rhs", None),
            P(None, "clu", None, None),
            P(None, "clu", None, None, None),
            P(None, "clu", None, None, None),
            P(None, "clu", None),
            P(None, "clu", None),
            P(None, "clu"),
        ),
        out_specs=P(None, "clu", "rhs", None),
        check_vma=False,
    )
```

```python
import jax
import jax.numpy as jnp
from jax import lax
from jax.sharding import PartitionSpec as P

LEVELS = 4


def gather_blocks(blocks, columns, table):
    dev_count = table.shape[0]
    present = columns >= 0
    safe = jnp.where(present, columns, 0)
    picked = table[safe % dev_count, safe // dev_count]
    picked = jnp.where(present[..., None, None], picked, jnp.zeros_like(picked))
    return jnp.sum(blocks[:, :, None, :, :] * picked[:, :, :, None, :], axis=(1, 4))


def solve_diag(inv_local, values):
    return jnp.sum(inv_local[:, None, :, :] * values[:, :, None, :], axis=3)


def per_device(rhs, inverse, lower_blocks, upper_blocks, lower_cols, upper_cols, levels):
    dev_count = lax.axis_size("clu")
    source = rhs[:, 0]
    inv_local = inverse[:, 0]
    low_local = lower_blocks[:, 0]
    up_local = upper_blocks[:, 0]
    low_cols = lower_cols[:, 0]
    up_cols = upper_cols[:, 0]
    sections = levels[:, 0]

    def share(values):
        spread = jnp.broadcast_to(values[None], (dev_count,) + values.shape)
        return lax.all_to_all(spread, "clu", 0, 0, tiled=False)

    forward = source
    for level_no in range(1, LEVELS):
        table = share(forward)
        update = source - gather_blocks(low_local, low_cols, table)
        forward = jnp.where((sections == level_no)[:, None, None], update, forward)
    backward = solve_diag(inv_local, forward)
    backward = jnp.where(
        (sections == LEVELS - 1)[:, None, None], backward, jnp.zeros_like(backward)
    )
    for level_no in range(LEVELS - 2, -1, -1):
        table = share(backward)
        update = solve_diag(inv_local, forward - gather_blocks(up_local, up_cols, table))
        backward = jnp.where((sections == level_no)[:, None, None], update, backward)
    return backward[:, None]


def solution(mesh):
    return jax.shard_map(
        per_device,
        mesh=mesh,
        in_specs=(
            P(None, "clu", "rhs", None),
            P(None, "clu", None, None),
            P(None, "clu", None, None, None),
            P(None, "clu", None, None, None),
            P(None, "clu", None),
            P(None, "clu", None),
            P(None, "clu"),
        ),
        out_specs=P(None, "clu", "rhs", None),
        check_vma=False,
    )
```

```python
import jax
import jax.numpy as jnp
from jax import lax
from jax.sharding import PartitionSpec as P

LEVELS = 4


def gather_blocks(blocks, columns, table):
    dev_count = table.shape[0]
    present = columns >= 0
    safe = jnp.where(present, columns, 0)
    flat = table.reshape(table.shape[0] * table.shape[1], -1)
    pos = (safe % dev_count) * table.shape[1] + safe // dev_count
    onehot = (pos[..., None] == jnp.arange(flat.shape[0])).astype(jnp.float32)
    picked = jnp.einsum("ckj,jx->ckx", onehot, flat, precision=lax.Precision.HIGHEST)
    picked = picked.reshape(columns.shape + table.shape[2:])
    picked = jnp.where(present[..., None, None], picked, jnp.zeros_like(picked))
    return jnp.sum(blocks[:, :, None, :, :] * picked[:, :, :, None, :], axis=(1, 4))


def solve_diag(inv_local, values):
    return jnp.sum(inv_local[:, None, :, :] * values[:, :, None, :], axis=3)


def per_device(rhs, inverse, lower_blocks, upper_blocks, lower_cols, upper_cols, levels):
    dev_count = lax.axis_size("clu")
    source = rhs[:, 0]
    inv_local = inverse[:, 0]
    low_local = lower_blocks[:, 0]
    up_local = upper_blocks[:, 0]
    low_cols = lower_cols[:, 0]
    up_cols = upper_cols[:, 0]
    sections = levels[:, 0]

    def share(values):
        spread = jnp.broadcast_to(values[None], (dev_count,) + values.shape)
        return lax.all_to_all(spread, "clu", 0, 0, tiled=False)

    forward = source
    for level_no in range(1, LEVELS):
        table = share(forward)
        update = source - gather_blocks(low_local, low_cols, table)
        forward = jnp.where((sections == level_no)[:, None, None], update, forward)
    backward = solve_diag(inv_local, forward)
    backward = jnp.where(
        (sections == LEVELS - 1)[:, None, None], backward, jnp.zeros_like(backward)
    )
    for level_no in range(LEVELS - 2, -1, -1):
        table = share(backward)
        update = solve_diag(inv_local, forward - gather_blocks(up_local, up_cols, table))
        backward = jnp.where((sections == level_no)[:, None, None], update, backward)
    return backward[:, None]


def solution(mesh):
    return jax.shard_map(
        per_device,
        mesh=mesh,
        in_specs=(
            P(None, "clu", "rhs", None),
            P(None, "clu", None, None),
            P(None, "clu", None, None, None),
            P(None, "clu", None, None, None),
            P(None, "clu", None),
            P(None, "clu", None),
            P(None, "clu"),
        ),
        out_specs=P(None, "clu", "rhs", None),
        check_vma=False,
    )
```

```python
import jax
import jax.numpy as jnp
from jax import lax
from jax.sharding import PartitionSpec as P

LEVELS = 4


def select_rows(columns, dev_count, local_count):
    present = columns >= 0
    safe = jnp.where(present, columns, 0)
    pos = (safe % dev_count) * local_count + safe // dev_count
    hit = (pos[..., None] == jnp.arange(dev_count * local_count)) & present[..., None]
    return hit.astype(jnp.float32)


def gather_blocks(blocks, selector, table):
    flat = table.reshape(table.shape[0] * table.shape[1], -1)
    picked = jnp.einsum("ckj,jx->ckx", selector, flat, precision=lax.Precision.HIGHEST)
    picked = picked.reshape(selector.shape[:2] + table.shape[2:])
    return jnp.sum(blocks[:, :, None, :, :] * picked[:, :, :, None, :], axis=(1, 4))


def solve_diag(inv_local, values):
    return jnp.sum(inv_local[:, None, :, :] * values[:, :, None, :], axis=3)


def per_device(rhs, inverse, lower_blocks, upper_blocks, lower_cols, upper_cols, levels):
    dev_count = lax.axis_size("clu")
    source = rhs[:, 0]
    inv_local = inverse[:, 0]
    low_local = lower_blocks[:, 0]
    up_local = upper_blocks[:, 0]
    sections = levels[:, 0]
    local_count = source.shape[0]
    low_sel = select_rows(lower_cols[:, 0], dev_count, local_count)
    up_sel = select_rows(upper_cols[:, 0], dev_count, local_count)

    def spread_of(values):
        return jnp.broadcast_to(values[None], (dev_count,) + values.shape)

    def share(spread):
        return lax.all_to_all(spread, "clu", 0, 0, tiled=False)

    first_table, low_sel, up_sel = lax.optimization_barrier(
        (share(spread_of(source)), low_sel, up_sel))
    forward = source
    spread = None
    for level_no in range(1, LEVELS):
        table = first_table if spread is None else share(spread)
        update = source - gather_blocks(low_local, low_sel, table)
        forward = jnp.where((sections == level_no)[:, None, None], update, forward)
        spread = spread_of(forward)
    backward = solve_diag(inv_local, forward)
    backward = jnp.where(
        (sections == LEVELS - 1)[:, None, None], backward, jnp.zeros_like(backward)
    )
    for level_no in range(LEVELS - 2, -1, -1):
        table = share(spread_of(backward))
        update = solve_diag(inv_local, forward - gather_blocks(up_local, up_sel, table))
        backward = jnp.where((sections == level_no)[:, None, None], update, backward)
    return backward[:, None]


def solution(mesh):
    return jax.shard_map(
        per_device,
        mesh=mesh,
        in_specs=(
            P(None, "clu", "rhs", None),
            P(None, "clu", None, None),
            P(None, "clu", None, None, None),
            P(None, "clu", None, None, None),
            P(None, "clu", None),
            P(None, "clu", None),
            P(None, "clu"),
        ),
        out_specs=P(None, "clu", "rhs", None),
        check_vma=False,
    )
```

```python
import jax
import jax.numpy as jnp
from jax import lax
from jax.sharding import PartitionSpec as P

LEVELS = 4


def select_rows(columns, dev_count, local_count):
    present = columns >= 0
    safe = jnp.where(present, columns, 0)
    pos = (safe % dev_count) * local_count + safe // dev_count
    hit = (pos[..., None] == jnp.arange(dev_count * local_count)) & present[..., None]
    return hit.astype(jnp.float32)


def gather_blocks(blocks, selector, table):
    flat = table.reshape(table.shape[0] * table.shape[1], -1)
    picked = jnp.einsum("ckj,jx->ckx", selector, flat, precision=lax.Precision.HIGHEST)
    picked = picked.reshape(selector.shape[:2] + table.shape[2:])
    return jnp.sum(blocks[:, :, None, :, :] * picked[:, :, :, None, :], axis=(1, 4))


def solve_diag(inv_local, values):
    return jnp.sum(inv_local[:, None, :, :] * values[:, :, None, :], axis=3)


def per_device(rhs, inverse, lower_blocks, upper_blocks, lower_cols, upper_cols, levels):
    dev_count = lax.axis_size("clu")
    source = rhs[:, 0]
    inv_local = inverse[:, 0]
    low_local = lower_blocks[:, 0]
    up_local = upper_blocks[:, 0]
    sections = levels[:, 0]
    local_count = source.shape[0]
    low_sel = select_rows(lower_cols[:, 0], dev_count, local_count)
    up_sel = select_rows(upper_cols[:, 0], dev_count, local_count)

    def spread_of(values):
        return jnp.broadcast_to(values[None], (dev_count,) + values.shape)

    def share(spread):
        return lax.all_to_all(spread, "clu", 0, 0, tiled=False)

    one = (lax.axis_index("clu") >= 0).astype(jnp.float32)
    first_table, low_sel, up_sel, low_local = lax.optimization_barrier(
        (share(spread_of(source)), low_sel, up_sel, low_local * one))
    forward = source
    spread = None
    for level_no in range(1, LEVELS):
        table = first_table if spread is None else share(spread)
        update = source - gather_blocks(low_local, low_sel, table)
        forward = jnp.where((sections == level_no)[:, None, None], update, forward)
        spread = spread_of(forward)
    backward = solve_diag(inv_local, forward)
    backward = jnp.where(
        (sections == LEVELS - 1)[:, None, None], backward, jnp.zeros_like(backward)
    )
    for level_no in range(LEVELS - 2, -1, -1):
        table = share(spread_of(backward))
        update = solve_diag(inv_local, forward - gather_blocks(up_local, up_sel, table))
        backward = jnp.where((sections == level_no)[:, None, None], update, backward)
    return backward[:, None]


def solution(mesh):
    return jax.shard_map(
        per_device,
        mesh=mesh,
        in_specs=(
            P(None, "clu", "rhs", None),
            P(None, "clu", None, None),
            P(None, "clu", None, None, None),
            P(None, "clu", None, None, None),
            P(None, "clu", None),
            P(None, "clu", None),
            P(None, "clu"),
        ),
        out_specs=P(None, "clu", "rhs", None),
        check_vma=False,
    )
```
